512 devices in a mesh: dp: 32 (over y, x, core), wide: 16 (over z).
Axes of the slice: x: 4, y: 4, z: 16, core: 2. Of those that a mesh axis runs over, the one named last changes fastest.
Arguments:
- trunk_out: bfloat16 [16384, 1024], P('dp'), may hold values from -6 to 6
- projection: bfloat16 [1024, 4096], P(None, 'wide'), may hold values from -0.1875 to 0.1875
- transform: bfloat16 [4096, 4096], P('wide'), may hold values from -0.125 to 0.125
- block_mask: int32 [32, 32], P('wide'), may hold values from 0 to 1, as said below
- old_index: bfloat16 [16384, 4096], P('dp', 'wide'), may hold values from -6 to 6
- doc_ids: int32 [16384, 4], P('dp'), may hold values from 0 to 16383, as said below
- labels: int32 [16384, 4], P('dp'), may hold values 0 or 1
Outputs:
- new_embed: bfloat16 [16384, 4096], P('dp', 'wide')
- pair_loss: float32 [16384, 4], P('dp')
- trunk_grad: bfloat16 [16384, 4096], P('dp', 'wide')
The draws below stay inside these ranges and needn't reach their ends.
Inputs may be any that keep to these rules, and one draw needn't show every extreme that they name: `doc_ids`: in each aligned block of 512 rows, no shard id // 512 is named more than 128 times, and one shard is named exactly 128 times. `block_mask`: each block row has 4 to 24 nonzero entries, and some block row has exactly 24.
All inputs are finite; a program needn't handle non-finite values. No bound on the sum of `labels` on one device may be relied on, other than what follows from the above.
Results may differ from the reference program's by a relative error of at most 0.015.
Values may be sent and summed in bfloat16 or wider, within the bound.
No kernel may reach another device: no remote copies, remote signals or barrier semaphores. Data moves between devices by JAX's collectives and lax.ppermute only.
A program may use at most 128 MiB of HBM per device.

```python
import math
import jax
import jax.numpy as jnp
from jax import lax

D = 1024
E = 4096
BLOCK = 128
NB = 32
MINB = 4
MAXB = 24
K = 4
ROWS = 512
DOC_SHARD = 512
TOKENS = 16384
OWNERS = 32
NDOC = 16384
CAP = 128
N_WIDE = 16


def draw_doc_ids(key, part):
    nblk = TOKENS // ROWS
    total = OWNERS * CAP
    count = ROWS * K

    def one_block(index):
        sub = jax.random.fold_in(jax.random.fold_in(key, 17), index)
        key_a, key_b, key_c, key_d = jax.random.split(sub, 4)
        slot_owner = jnp.arange(total, dtype=jnp.int32) // CAP
        ranks = jax.random.permutation(key_a, total).astype(jnp.int32)
        forced = jax.random.randint(key_b, (), 0, OWNERS, dtype=jnp.int32)
        order_key = jnp.where(slot_owner == forced, -1, ranks)
        order = jnp.argsort(order_key, stable=True)
        owners = slot_owner[order][:count]
        owners = owners[jax.random.permutation(key_c, count)]
        local = jax.random.randint(key_d, (count,), 0, DOC_SHARD, dtype=jnp.int32)
        return (owners * DOC_SHARD + local).reshape(ROWS, K)
    return jax.vmap(one_block)(jnp.arange(nblk, dtype=jnp.int32)).reshape(TOKENS, K)


def draw_block_mask(key, part):
    key_a, key_b, key_c = jax.random.split(jax.random.fold_in(key, 29), 3)
    counts = jax.random.randint(key_a, (NB,), MINB, MAXB + 1, dtype=jnp.int32)
    top_row = jax.random.randint(key_b, (), 0, NB, dtype=jnp.int32)
    counts = jnp.where(jnp.arange(NB, dtype=jnp.int32) == top_row, MAXB, counts)
    perms = jax.vmap(lambda sub: jax.random.permutation(sub, NB).astype(jnp.int32))(jax.random.split(key_c, NB))
    return (perms < counts[:, None]).astype(jnp.int32)


def with_ends(values, stream_key, least, largest):
    longest = values.shape.index(max(values.shape))
    spots = []
    for shift in (0, 1):
        where = [jax.random.randint(jax.random.fold_in(stream_key, axis), (), 0, length) for axis, length in enumerate(values.shape)]
        where[longest] = (where[longest] + shift) % values.shape[longest]
        spots.append(tuple(where))
    return values.at[spots[0]].set(least).at[spots[1]].set(largest)


def steps_of(rng, dims, cuts, least, high):
    factor_of = 1.0
    for position, shards_of in cuts:
        steps = jax.random.uniform(jax.random.fold_in(jax.random.fold_in(rng, 6), position), (shards_of,), jnp.float32, least / len(cuts), high / len(cuts))
        factor_of = factor_of * jnp.repeat(jnp.exp(steps), dims[position] // shards_of).reshape((-1,) + (1,) * (len(dims) - 1 - position))
    return factor_of


def scatter_about(key, extent, spread, most, shards=(), kind=jnp.bfloat16):
    loudness = steps_of(key, extent, shards, -0.22, 0.18) if shards else 1.0
    values = jax.random.normal(key, extent, jnp.float32) * spread * loudness
    return jnp.minimum(jnp.maximum(values, -most), most).astype(kind)


def setup_inputs(seed: int = 0) -> dict:
    seeds = jax.random.split(jax.random.key(seed), 8)
    return {
        "trunk_out": scatter_about(seeds[0], (TOKENS, D), 1.0, 6.0, ((0, 32),)),
        "projection": scatter_about(seeds[1], (D, E), D ** -0.5, 0.1875, ((1, 16),)),
        "transform": scatter_about(seeds[2], (E, E), (E * (MINB + MAXB) // (2 * NB)) ** -0.5, 0.125, ((0, 16),)),
        "block_mask": draw_block_mask(jax.random.fold_in(seeds[7], 71), 0),
        "old_index": scatter_about(seeds[4], (NDOC, E), 1.0, 6.0, ((0, 32), (1, 16))),
        "doc_ids": draw_doc_ids(jax.random.fold_in(seeds[7], 71), 0),
        "labels": with_ends((jax.random.randint(seeds[6], (TOKENS, K), 0, 2) < 1).astype(jnp.int32), jax.random.fold_in(seeds[6], 1), 0, 1),
    }


def reference(trunk_out, projection, transform, block_mask, old_index, doc_ids, labels):
    query = jnp.dot(trunk_out, projection, preferred_element_type=jnp.float32).astype(jnp.bfloat16)
    nblocks = E // BLOCK
    masked = (transform.reshape(nblocks, BLOCK, nblocks, BLOCK) * block_mask[:, None, :, None].astype(jnp.bfloat16)).reshape(E, E)
    group = E // N_WIDE

    def add_group(index, total):
        start = index * group
        q_part = lax.dynamic_slice_in_dim(query, start, group, 1)
        m_part = lax.dynamic_slice_in_dim(masked, start, group, 0)
        partial_value = jnp.dot(q_part, m_part, preferred_element_type=jnp.float32)
        return total + lax.optimization_barrier(partial_value.astype(jnp.bfloat16)).astype(jnp.float32)
    new = lax.fori_loop(0, N_WIDE, add_group, jnp.zeros((TOKENS, E), jnp.float32))
    scale = 1.0 / math.sqrt(E)
    nblk = TOKENS // ROWS

    def score_block(args):
        new_blk, ids_blk, lab_blk = args
        old_vec = old_index[ids_blk].astype(jnp.float32)
        score = jnp.einsum('re,rke->rk', new_blk, old_vec) * scale
        sign = 2.0 * lab_blk.astype(jnp.float32) - 1.0
        loss = jax.nn.softplus(-sign * score)
        dscore = -sign * jax.nn.sigmoid(-sign * score)
        grad_new = (jnp.einsum('rk,rke->re', dscore, old_vec) * scale).astype(jnp.bfloat16)
        return (loss, grad_new)
    loss, grad_new = lax.map(score_block, (new.reshape(nblk, ROWS, E), doc_ids.reshape(nblk, ROWS, K), labels.reshape(nblk, ROWS, K)))
    pair_loss = loss.reshape(TOKENS, K)
    grad_new = grad_new.reshape(TOKENS, E)
    trunk_grad = lax.dot_general(grad_new, masked, (((1,), (1,)), ((), ())), preferred_element_type=jnp.float32).astype(jnp.bfloat16)
    return (new.astype(jnp.bfloat16), pair_loss, trunk_grad)
```

```python
import math

import jax
import jax.numpy as jnp
from jax import lax
from jax.sharding import PartitionSpec as P

E = 4096
K = 4
CAP = 128


def local(n_dp, trunk_out, projection, transform, block_mask, old_index, doc_ids, labels):
    rows, dmodel = trunk_out.shape
    e_local, width = transform.shape
    local_blocks, nblocks = block_mask.shape
    side = e_local // local_blocks
    doc_shard = old_index.shape[0]
    blocks = transform.reshape(local_blocks, side, nblocks, side)
    masked = (blocks * block_mask[:, None, :, None].astype(jnp.bfloat16)).reshape(e_local, width)

    chunk = dmodel // n_dp
    me = lax.axis_index("dp")
    proj_rows = lax.dynamic_slice_in_dim(projection, me * chunk, chunk, 0)
    w_part = jnp.dot(proj_rows, masked, preferred_element_type=jnp.float32)
    w_blk = lax.psum_scatter(w_part, "wide", scatter_dimension=1, tiled=True)
    w_cols = lax.all_gather(w_blk.astype(jnp.bfloat16), "dp", axis=0, tiled=True)
    new = jnp.dot(trunk_out, w_cols, preferred_element_type=jnp.float32)

    flat = doc_ids.reshape(-1)
    owner = flat // doc_shard
    loc = flat - owner * doc_shard
    onehot = (owner[:, None] == jnp.arange(n_dp, dtype=jnp.int32)[None, :]).astype(jnp.int32)
    before = jnp.cumsum(onehot, axis=0) - onehot
    rank = jnp.sum(before * onehot, axis=1)
    slot = owner * CAP + rank
    req = jnp.zeros((n_dp * CAP,), jnp.int32).at[slot].set(loc, unique_indices=True)
    asked = lax.all_to_all(req.reshape(n_dp, CAP), "dp", 0, 0, tiled=True)
    served = old_index[asked.reshape(-1)].reshape(n_dp, CAP, e_local)
    back = lax.all_to_all(served, "dp", 0, 0, tiled=True).reshape(n_dp * CAP, e_local)
    old_vec = back[slot].reshape(rows, K, e_local)

    old_wide = old_vec.astype(jnp.float32)
    scale = 1.0 / math.sqrt(E)
    partial_scores = jnp.einsum("re,rke->rk", new, old_wide)
    score = lax.psum(partial_scores, "wide") * scale
    sign = 2.0 * labels.astype(jnp.float32) - 1.0
    pair_loss = jax.nn.softplus(-sign * score)
    dscore = -sign * jax.nn.sigmoid(-sign * score)
    grad_local = (jnp.einsum("rk,rke->re", dscore, old_wide) * scale).astype(jnp.bfloat16)
    grad_full = lax.all_gather(grad_local, "wide", axis=1, tiled=True)
    trunk_grad = lax.dot_general(
        grad_full, masked, (((1,), (1,)), ((), ())), preferred_element_type=jnp.float32
    )
    return (new.astype(jnp.bfloat16), pair_loss, trunk_grad.astype(jnp.bfloat16))


def solution(mesh):
    n_dp = mesh.shape["dp"]
    return jax.shard_map(
        lambda *a: local(n_dp, *a),
        mesh=mesh,
        in_specs=(
            P("dp", None),
            P(None, "wide"),
            P("wide", None),
            P("wide", None),
            P("dp", "wide"),
            P("dp", None),
            P("dp", None),
        ),
        out_specs=(P("dp", "wide"), P("dp", None), P("dp", "wide")),
        check_vma=False,
    )
```

```python
import math

import jax
import jax.numpy as jnp
from jax import lax
from jax.sharding import PartitionSpec as P

E = 4096
K = 4
CAP = 128


def one_hot(index, size, dtype=jnp.bfloat16):
    return (index[:, None] == jnp.arange(size, dtype=jnp.int32)[None, :]).astype(dtype)


def pick_rows(index, table):
    picked = jnp.dot(one_hot(index, table.shape[0]), table, preferred_element_type=jnp.float32)
    return picked.astype(table.dtype)


def local(n_dp, n_wide, trunk_out, projection, transform, block_mask, old_index, doc_ids, labels):
    rows = trunk_out.shape[0]
    e_local, width = transform.shape
    local_blocks, nblocks = block_mask.shape
    side = e_local // local_blocks
    doc_shard = old_index.shape[0]
    query = jnp.dot(trunk_out, projection, preferred_element_type=jnp.float32).astype(jnp.bfloat16)
    blocks = transform.reshape(local_blocks, side, nblocks, side)
    masked = (blocks * block_mask[:, None, :, None].astype(jnp.bfloat16)).reshape(e_local, width)
    term = jnp.dot(query, masked, preferred_element_type=jnp.float32)
    new = lax.psum_scatter(
        term.astype(jnp.bfloat16), "wide", scatter_dimension=1, tiled=True
    ).astype(jnp.float32)

    flat = doc_ids.reshape(-1)
    count = flat.shape[0]
    owner = flat // doc_shard
    loc = flat - owner * doc_shard
    by_owner = one_hot(owner, n_dp)
    ids = jnp.arange(count, dtype=jnp.int32)
    earlier = (ids[None, :] < ids[:, None]).astype(jnp.bfloat16)
    before = jnp.dot(earlier, by_owner, preferred_element_type=jnp.float32)
    rank = jnp.sum(before * by_owner.astype(jnp.float32), axis=1).astype(jnp.int32)
    slot = owner * CAP + rank
    by_rank = one_hot(rank, CAP)
    digits = jnp.stack([loc // 32, loc % 32], axis=0).astype(jnp.bfloat16)
    placed = jnp.einsum("di,io,ic->doc", digits, by_owner, by_rank,
                        preferred_element_type=jnp.float32).astype(jnp.int32)
    req = placed[0] * 32 + placed[1]
    asked = lax.all_to_all(req, "dp", 0, 0, tiled=True)
    served = pick_rows(asked.reshape(-1), old_index).reshape(n_dp, CAP, e_local)
    back = lax.all_to_all(served, "dp", 0, 0, tiled=True).reshape(n_dp * CAP, e_local)
    old_vec = pick_rows(slot, back).reshape(rows, K, e_local)

    old_wide = old_vec.astype(jnp.float32)
    scale = 1.0 / math.sqrt(E)
    partial_scores = jnp.einsum("re,rke->rk", new, old_wide)
    spread = jnp.broadcast_to(partial_scores[None], (n_wide,) + partial_scores.shape)
    gathered = lax.all_to_all(spread, "wide", 0, 0, tiled=True)
    score = jnp.sum(gathered, axis=0) * scale
    sign = 2.0 * labels.astype(jnp.float32) - 1.0
    pair_loss = jax.nn.softplus(-sign * score)
    dscore = -sign * jax.nn.sigmoid(-sign * score)
    grad_local = (jnp.einsum("rk,rke->re", dscore, old_wide) * scale).astype(jnp.bfloat16)
    grad_full = lax.all_gather(grad_local, "wide", axis=1, tiled=True)
    trunk_grad = lax.dot_general(
        grad_full, masked, (((1,), (1,)), ((), ())), preferred_element_type=jnp.float32
    )
    return (new.astype(jnp.bfloat16), pair_loss, trunk_grad.astype(jnp.bfloat16))


def solution(mesh):
    n_dp, n_wide = mesh.shape["dp"], mesh.shape["wide"]
    return jax.shard_map(
        lambda *a: local(n_dp, n_wide, *a),
        mesh=mesh,
        in_specs=(
            P("dp", None),
            P(None, "wide"),
            P("wide", None),
            P("wide", None),
            P("dp", "wide"),
            P("dp", None),
            P("dp", None),
        ),
        out_specs=(P("dp", "wide"), P("dp", None), P("dp", "wide")),
        check_vma=False,
    )
```

```python
import math

import jax
import jax.numpy as jnp
from jax import lax
from jax.sharding import PartitionSpec as P

E = 4096
K = 4
CAP = 128


def one_hot(index, size, dtype=jnp.bfloat16):
    return (index[:, None] == jnp.arange(size, dtype=jnp.int32)[None, :]).astype(dtype)


def pick_rows(index, table):
    picked = jnp.dot(one_hot(index, table.shape[0]), table, preferred_element_type=jnp.float32)
    return picked.astype(table.dtype)


def local(n_dp, n_wide, trunk_out, projection, transform, block_mask, old_index, doc_ids, labels):
    rows = trunk_out.shape[0]
    e_local, width = transform.shape
    local_blocks, nblocks = block_mask.shape
    side = e_local // local_blocks
    doc_shard = old_index.shape[0]
    query = jnp.dot(trunk_out, projection, preferred_element_type=jnp.float32).astype(jnp.bfloat16)
    blocks = transform.reshape(local_blocks, side, nblocks, side)
    masked = (blocks * block_mask[:, None, :, None].astype(jnp.bfloat16)).reshape(e_local, width)
    term = jnp.dot(query, masked, preferred_element_type=jnp.float32)
    new = lax.psum_scatter(
        term.astype(jnp.bfloat16), "wide", scatter_dimension=1, tiled=True
    ).astype(jnp.float32)

    flat = doc_ids.reshape(-1)
    count = flat.shape[0]
    owner = flat // doc_shard
    loc = flat - owner * doc_shard
    by_owner = one_hot(owner, n_dp)
    ids = jnp.arange(count, dtype=jnp.int32)
    earlier = (ids[None, :] < ids[:, None]).astype(jnp.bfloat16)
    before = jnp.dot(earlier, by_owner, preferred_element_type=jnp.float32)
    rank = jnp.sum(before * by_owner.astype(jnp.float32), axis=1).astype(jnp.int32)
    slot = owner * CAP + rank
    by_rank = one_hot(rank, CAP)
    digits = jnp.stack([loc // 32, loc % 32], axis=0).astype(jnp.bfloat16)
    placed = jnp.einsum("di,io,ic->doc", digits, by_owner, by_rank,
                        preferred_element_type=jnp.float32).astype(jnp.int32)
    req = placed[0] * 32 + placed[1]
    asked = lax.all_to_all(req, "dp", 0, 0, tiled=True).reshape(-1)
    served = pick_rows(asked, old_index).reshape(n_dp, CAP, e_local)
    back = lax.all_to_all(served, "dp", 0, 0, tiled=True).reshape(n_dp * CAP, e_local)
    old_vec = pick_rows(slot, back).reshape(rows, K, e_local)

    old_full = lax.all_gather(old_index, "wide", axis=1, tiled=True)
    g_own = lax.dot_general(
        old_full, masked, (((1,), (1,)), ((), ())), preferred_element_type=jnp.float32
    ).astype(jnp.bfloat16)
    served_g = pick_rows(asked, g_own).reshape(n_dp, CAP, e_local)
    back_g = lax.all_to_all(served_g, "dp", 0, 0, tiled=True).reshape(n_dp * CAP, e_local)
    g_vec = pick_rows(slot, back_g).reshape(rows, K, e_local).astype(jnp.float32)

    old_wide = old_vec.astype(jnp.float32)
    scale = 1.0 / math.sqrt(E)
    partial_scores = jnp.einsum("re,rke->rk", new, old_wide)
    spread = jnp.broadcast_to(partial_scores[None], (n_wide,) + partial_scores.shape)
    gathered = lax.all_to_all(spread, "wide", 0, 0, tiled=True)
    score = jnp.sum(gathered, axis=0) * scale
    sign = 2.0 * labels.astype(jnp.float32) - 1.0
    pair_loss = jax.nn.softplus(-sign * score)
    dscore = -sign * jax.nn.sigmoid(-sign * score)
    trunk_grad = jnp.einsum("rk,rke->re", dscore, g_vec) * scale
    return (new.astype(jnp.bfloat16), pair_loss, trunk_grad.astype(jnp.bfloat16))


def solution(mesh):
    n_dp, n_wide = mesh.shape["dp"], mesh.shape["wide"]
    return jax.shard_map(
        lambda *a: local(n_dp, n_wide, *a),
        mesh=mesh,
        in_specs=(
            P("dp", None),
            P(None, "wide"),
            P("wide", None),
            P("wide", None),
            P("dp", "wide"),
            P("dp", None),
            P("dp", None),
        ),
        out_specs=(P("dp", "wide"), P("dp", None), P("dp", "wide")),
        check_vma=False,
    )
```

```python
import math

import jax
import jax.numpy as jnp
from jax import lax
from jax.sharding import PartitionSpec as P

E = 4096
K = 4
CAP = 128


def one_hot(index, size, dtype=jnp.bfloat16):
    return (index[:, None] == jnp.arange(size, dtype=jnp.int32)[None, :]).astype(dtype)


def pick_rows(index, table):
    picked = jnp.dot(one_hot(index, table.shape[0]), table, preferred_element_type=jnp.float32)
    return picked.astype(table.dtype)


def local(n_dp, n_wide, trunk_out, projection, transform, block_mask, old_index, doc_ids, labels):
    rows = trunk_out.shape[0]
    e_local, width = transform.shape
    local_blocks, nblocks = block_mask.shape
    side = e_local // local_blocks
    doc_shard = old_index.shape[0]
    query = jnp.dot(trunk_out, projection, preferred_element_type=jnp.float32).astype(jnp.bfloat16)
    blocks = transform.reshape(local_blocks, side, nblocks, side)
    masked = (blocks * block_mask[:, None, :, None].astype(jnp.bfloat16)).reshape(e_local, width)
    term = jnp.dot(query, masked, preferred_element_type=jnp.float32)
    new = lax.psum_scatter(
        term.astype(jnp.bfloat16), "wide", scatter_dimension=1, tiled=True
    ).astype(jnp.float32)

    flat = doc_ids.reshape(-1)
    count = flat.shape[0]
    owner = flat // doc_shard
    loc = flat - owner * doc_shard
    by_owner = one_hot(owner, n_dp)
    ids = jnp.arange(count, dtype=jnp.int32)
    earlier = (ids[None, :] < ids[:, None]).astype(jnp.bfloat16)
    before = jnp.dot(earlier, by_owner, preferred_element_type=jnp.float32)
    rank = jnp.sum(before * by_owner.astype(jnp.float32), axis=1).astype(jnp.int32)
    slot = owner * CAP + rank
    by_rank = one_hot(rank, CAP)
    digits = jnp.stack([loc // 32, loc % 32], axis=0).astype(jnp.bfloat16)
    placed = jnp.einsum("di,io,ic->doc", digits, by_owner, by_rank,
                        preferred_element_type=jnp.float32).astype(jnp.int32)
    req = placed[0] * 32 + placed[1]
    asked = lax.all_to_all(req, "dp", 0, 0, tiled=True).reshape(-1)
    served = pick_rows(asked, old_index).reshape(n_dp, CAP, e_local)
    back = lax.all_to_all(served, "dp", 0, 0, tiled=True).reshape(n_dp * CAP, e_local)
    old_vec = pick_rows(slot, back).reshape(rows, K, e_local)

    me_w = lax.axis_index("wide")
    right = [(i, (i + 1) % n_wide) for i in range(n_wide)]
    left = [(i, (i - 1) % n_wide) for i in range(n_wide)]

    def place(full, block, source):
        return lax.dynamic_update_slice_in_dim(full, block, source * e_local, 1)

    old_full = place(jnp.zeros((doc_shard, width), old_index.dtype), old_index, me_w)
    to_right, to_left = old_index, old_index
    for step in range(1, n_wide // 2 + 1):
        to_right = lax.ppermute(to_right, "wide", right)
        old_full = place(old_full, to_right, (me_w - step) % n_wide)
        if step < n_wide - n_wide // 2:
            to_left = lax.ppermute(to_left, "wide", left)
            old_full = place(old_full, to_left, (me_w + step) % n_wide)
    g_own = lax.dot_general(
        old_full, masked, (((1,), (1,)), ((), ())), preferred_element_type=jnp.float32
    ).astype(jnp.bfloat16)
    served_g = pick_rows(asked, g_own).reshape(n_dp, CAP, e_local)
    back_g = lax.all_to_all(served_g, "dp", 0, 0, tiled=True).reshape(n_dp * CAP, e_local)
    g_vec = pick_rows(slot, back_g).reshape(rows, K, e_local).astype(jnp.float32)

    old_wide = old_vec.astype(jnp.float32)
    scale = 1.0 / math.sqrt(E)
    partial_scores = jnp.einsum("re,rke->rk", new, old_wide)
    spread = jnp.broadcast_to(partial_scores[None], (n_wide,) + partial_scores.shape)
    gathered = lax.all_to_all(spread, "wide", 0, 0, tiled=True)
    score = jnp.sum(gathered, axis=0) * scale
    sign = 2.0 * labels.astype(jnp.float32) - 1.0
    pair_loss = jax.nn.softplus(-sign * score)
    dscore = -sign * jax.nn.sigmoid(-sign * score)
    trunk_grad = jnp.einsum("rk,rke->re", dscore, g_vec) * scale
    return (new.astype(jnp.bfloat16), pair_loss, trunk_grad.astype(jnp.bfloat16))


def solution(mesh):
    n_dp, n_wide = mesh.shape["dp"], mesh.shape["wide"]
    return jax.shard_map(
        lambda *a: local(n_dp, n_wide, *a),
        mesh=mesh,
        in_specs=(
            P("dp", None),
            P(None, "wide"),
            P("wide", None),
            P("wide", None),
            P("dp", "wide"),
            P("dp", None),
            P("dp", None),
        ),
        out_specs=(P("dp", "wide"), P("dp", None), P("dp", "wide")),
        check_vma=False,
    )
```

```python
import math

import jax
import jax.numpy as jnp
from jax import lax
from jax.sharding import PartitionSpec as P

E = 4096
K = 4
CAP = 128


def one_hot(index, size, dtype=jnp.bfloat16):
    return (index[:, None] == jnp.arange(size, dtype=jnp.int32)[None, :]).astype(dtype)


def pick_rows(index, table):
    picked = jnp.dot(one_hot(index, table.shape[0]), table, preferred_element_type=jnp.float32)
    return picked.astype(table.dtype)


def local(n_dp, n_wide, trunk_out, projection, transform, block_mask, old_index, doc_ids, labels):
    rows = trunk_out.shape[0]
    e_local, width = transform.shape
    local_blocks, nblocks = block_mask.shape
    side = e_local // local_blocks
    doc_shard = old_index.shape[0]
    query = jnp.dot(trunk_out, projection, preferred_element_type=jnp.float32).astype(jnp.bfloat16)
    blocks = transform.reshape(local_blocks, side, nblocks, side)
    masked = (blocks * block_mask[:, None, :, None].astype(jnp.bfloat16)).reshape(e_local, width)
    term = jnp.dot(query, masked, preferred_element_type=jnp.float32)
    new = lax.psum_scatter(
        term.astype(jnp.bfloat16), "wide", scatter_dimension=1, tiled=True
    ).astype(jnp.float32)

    flat = doc_ids.reshape(-1)
    count = flat.shape[0]
    owner = flat // doc_shard
    loc = flat - owner * doc_shard
    by_owner = one_hot(owner, n_dp)
    ids = jnp.arange(count, dtype=jnp.int32)
    earlier = (ids[None, :] < ids[:, None]).astype(jnp.bfloat16)
    before = jnp.dot(earlier, by_owner, preferred_element_type=jnp.float32)
    rank = jnp.sum(before * by_owner.astype(jnp.float32), axis=1).astype(jnp.int32)
    slot = owner * CAP + rank
    by_rank = one_hot(rank, CAP)
    digits = jnp.stack([loc // 32, loc % 32], axis=0).astype(jnp.bfloat16)
    placed = jnp.einsum("di,io,ic->doc", digits, by_owner, by_rank,
                        preferred_element_type=jnp.float32).astype(jnp.int32)
    req = placed[0] * 32 + placed[1]
    asked = lax.all_to_all(req, "dp", 0, 0, tiled=True).reshape(-1)
    served = pick_rows(asked, old_index).reshape(n_dp, CAP, e_local)
    back = lax.all_to_all(served, "dp", 0, 0, tiled=True).reshape(n_dp * CAP, e_local)
    old_vec = pick_rows(slot, back).reshape(rows, K, e_local)

    me_w = lax.axis_index("wide")
    right = [(i, (i + 1) % n_wide) for i in range(n_wide)]
    left = [(i, (i - 1) % n_wide) for i in range(n_wide)]

    def place(full, block, source):
        return lax.dynamic_update_slice_in_dim(full, block, source * e_local, 1)

    old_full = place(jnp.zeros((doc_shard, width), old_index.dtype), old_index, me_w)
    to_right, to_left = old_index, old_index
    for step in range(1, n_wide // 2 + 1):
        to_right = lax.ppermute(to_right, "wide", right)
        old_full = place(old_full, to_right, (me_w - step) % n_wide)
        if step < n_wide - n_wide // 2:
            to_left = lax.ppermute(to_left, "wide", left)
            old_full = place(old_full, to_left, (me_w + step) % n_wide)
    g_own = lax.dot_general(
        old_full, masked, (((1,), (1,)), ((), ())), preferred_element_type=jnp.float32
    ).astype(jnp.bfloat16)

    old_wide = old_vec.astype(jnp.float32)
    scale = 1.0 / math.sqrt(E)
    partial_scores = jnp.einsum("re,rke->rk", new, old_wide)
    spread = jnp.broadcast_to(partial_scores[None], (n_wide,) + partial_scores.shape)
    gathered = lax.all_to_all(spread, "wide", 0, 0, tiled=True)
    g_own, gathered = lax.optimization_barrier((g_own, gathered))
    served_g = pick_rows(asked, g_own).reshape(n_dp, CAP, e_local)
    back_g = lax.all_to_all(served_g, "dp", 0, 0, tiled=True).reshape(n_dp * CAP, e_local)
    g_vec = pick_rows(slot, back_g).reshape(rows, K, e_local).astype(jnp.float32)
    score = jnp.sum(gathered, axis=0) * scale
    sign = 2.0 * labels.astype(jnp.float32) - 1.0
    pair_loss = jax.nn.softplus(-sign * score)
    dscore = -sign * jax.nn.sigmoid(-sign * score)
    trunk_grad = jnp.einsum("rk,rke->re", dscore, g_vec) * scale
    return (new.astype(jnp.bfloat16), pair_loss, trunk_grad.astype(jnp.bfloat16))


def solution(mesh):
    n_dp, n_wide = mesh.shape["dp"], mesh.shape["wide"]
    return jax.shard_map(
        lambda *a: local(n_dp, n_wide, *a),
        mesh=mesh,
        in_specs=(
            P("dp", None),
            P(None, "wide"),
            P("wide", None),
            P("wide", None),
            P("dp", "wide"),
            P("dp", None),
            P("dp", None),
        ),
        out_specs=(P("dp", "wide"), P("dp", None), P("dp", "wide")),
        check_vma=False,
    )
```

```python
import math

import jax
import jax.numpy as jnp
from jax import lax
from jax.sharding import PartitionSpec as P

E = 4096
K = 4
CAP = 128


def one_hot(index, size, dtype=jnp.bfloat16):
    return (index[:, None] == jnp.arange(size, dtype=jnp.int32)[None, :]).astype(dtype)


def pick_rows(index, table):
    picked = jnp.dot(one_hot(index, table.shape[0]), table, preferred_element_type=jnp.float32)
    return picked.astype(table.dtype)


def local(n_dp, n_wide, trunk_out, projection, transform, block_mask, old_index, doc_ids, labels):
    rows = trunk_out.shape[0]
    e_local, width = transform.shape
    local_blocks, nblocks = block_mask.shape
    side = e_local // local_blocks
    doc_shard = old_index.shape[0]
    blocks = transform.reshape(local_blocks, side, nblocks, side)
    masked = (blocks * block_mask[:, None, :, None].astype(jnp.bfloat16)).reshape(e_local, width)

    dmodel = trunk_out.shape[1]
    chunk = dmodel // n_dp
    proj_rows = lax.dynamic_slice_in_dim(projection, lax.axis_index("dp") * chunk, chunk, 0)
    w_part = jnp.dot(proj_rows, masked, preferred_element_type=jnp.float32)
    w_blk = lax.psum_scatter(w_part, "wide", scatter_dimension=1, tiled=True)
    w_cols = lax.all_gather(w_blk.astype(jnp.bfloat16), "dp", axis=0, tiled=True)
    new = jnp.dot(trunk_out, w_cols, preferred_element_type=jnp.float32)

    flat = doc_ids.reshape(-1)
    count = flat.shape[0]
    owner = flat // doc_shard
    loc = flat - owner * doc_shard
    by_owner = one_hot(owner, n_dp)
    ids = jnp.arange(count, dtype=jnp.int32)
    earlier = (ids[None, :] < ids[:, None]).astype(jnp.bfloat16)
    before = jnp.dot(earlier, by_owner, preferred_element_type=jnp.float32)
    rank = jnp.sum(before * by_owner.astype(jnp.float32), axis=1).astype(jnp.int32)
    slot = owner * CAP + rank
    by_rank = one_hot(rank, CAP)
    digits = jnp.stack([loc // 32, loc % 32], axis=0).astype(jnp.bfloat16)
    placed = jnp.einsum("di,io,ic->doc", digits, by_owner, by_rank,
                        preferred_element_type=jnp.float32).astype(jnp.int32)
    req = placed[0] * 32 + placed[1]
    asked = lax.all_to_all(req, "dp", 0, 0, tiled=True).reshape(-1)
    served = pick_rows(asked, old_index).reshape(n_dp, CAP, e_local)
    back = lax.all_to_all(served, "dp", 0, 0, tiled=True).reshape(n_dp * CAP, e_local)
    old_vec = pick_rows(slot, back).reshape(rows, K, e_local)

    me_w = lax.axis_index("wide")
    right = [(i, (i + 1) % n_wide) for i in range(n_wide)]
    left = [(i, (i - 1) % n_wide) for i in range(n_wide)]

    def place(full, block, source):
        return lax.dynamic_update_slice_in_dim(full, block, source * e_local, 1)

    old_full = place(jnp.zeros((doc_shard, width), old_index.dtype), old_index, me_w)
    to_right, to_left = old_index, old_index
    for step in range(1, n_wide // 2 + 1):
        to_right = lax.ppermute(to_right, "wide", right)
        old_full = place(old_full, to_right, (me_w - step) % n_wide)
        if step < n_wide - n_wide // 2:
            to_left = lax.ppermute(to_left, "wide", left)
            old_full = place(old_full, to_left, (me_w + step) % n_wide)
    g_own = lax.dot_general(
        old_full, masked, (((1,), (1,)), ((), ())), preferred_element_type=jnp.float32
    ).astype(jnp.bfloat16)
    served_g = pick_rows(asked, g_own).reshape(n_dp, CAP, e_local)
    back_g = lax.all_to_all(served_g, "dp", 0, 0, tiled=True).reshape(n_dp * CAP, e_local)
    g_vec = pick_rows(slot, back_g).reshape(rows, K, e_local).astype(jnp.float32)

    old_wide = old_vec.astype(jnp.float32)
    scale = 1.0 / math.sqrt(E)
    partial_scores = jnp.einsum("re,rke->rk", new, old_wide)
    spread = jnp.broadcast_to(partial_scores[None], (n_wide,) + partial_scores.shape)
    gathered = lax.all_to_all(spread, "wide", 0, 0, tiled=True)
    score = jnp.sum(gathered, axis=0) * scale
    sign = 2.0 * labels.astype(jnp.float32) - 1.0
    pair_loss = jax.nn.softplus(-sign * score)
    dscore = -sign * jax.nn.sigmoid(-sign * score)
    trunk_grad = jnp.einsum("rk,rke->re", dscore, g_vec) * scale
    return (new.astype(jnp.bfloat16), pair_loss, trunk_grad.astype(jnp.bfloat16))


def solution(mesh):
    n_dp, n_wide = mesh.shape["dp"], mesh.shape["wide"]
    return jax.shard_map(
        lambda *a: local(n_dp, n_wide, *a),
        mesh=mesh,
        in_specs=(
            P("dp", None),
            P(None, "wide"),
            P("wide", None),
            P("wide", None),
            P("dp", "wide"),
            P("dp", None),
            P("dp", None),
        ),
        out_specs=(P("dp", "wide"), P("dp", None), P("dp", "wide")),
        check_vma=False,
    )
```

```python
import math

import jax
import jax.numpy as jnp
from jax import lax
from jax.sharding import PartitionSpec as P

E = 4096
K = 4
CAP = 128


def one_hot(index, size, dtype=jnp.bfloat16):
    return (index[:, None] == jnp.arange(size, dtype=jnp.int32)[None, :]).astype(dtype)


def pick_rows(index, table):
    picked = jnp.dot(one_hot(index, table.shape[0]), table, preferred_element_type=jnp.float32)
    return picked.astype(table.dtype)


def local(n_dp, n_wide, trunk_out, projection, transform, block_mask, old_index, doc_ids, labels):
    rows = trunk_out.shape[0]
    e_local, width = transform.shape
    local_blocks, nblocks = block_mask.shape
    side = e_local // local_blocks
    doc_shard = old_index.shape[0]
    query = jnp.dot(trunk_out, projection, preferred_element_type=jnp.float32).astype(jnp.bfloat16)
    blocks = transform.reshape(local_blocks, side, nblocks, side)
    masked = (blocks * block_mask[:, None, :, None].astype(jnp.bfloat16)).reshape(e_local, width)
    term = jnp.dot(query, masked, preferred_element_type=jnp.float32)
    new = lax.psum_scatter(
        term.astype(jnp.bfloat16), "wide", scatter_dimension=1, tiled=True
    ).astype(jnp.float32)

    flat = doc_ids.reshape(-1)
    count = flat.shape[0]
    owner = flat // doc_shard
    loc = flat - owner * doc_shard
    by_owner = one_hot(owner, n_dp)
    ids = jnp.arange(count, dtype=jnp.int32)
    earlier = (ids[None, :] < ids[:, None]).astype(jnp.bfloat16)
    before = jnp.dot(earlier, by_owner, preferred_element_type=jnp.float32)
    rank = jnp.sum(before * by_owner.astype(jnp.float32), axis=1).astype(jnp.int32)
    slot = owner * CAP + rank
    by_rank = one_hot(rank, CAP)
    digits = jnp.stack([loc // 32, loc % 32], axis=0).astype(jnp.bfloat16)
    placed = jnp.einsum("di,io,ic->doc", digits, by_owner, by_rank,
                        preferred_element_type=jnp.float32).astype(jnp.int32)
    req = placed[0] * 32 + placed[1]
    asked = lax.all_to_all(req, "dp", 0, 0, tiled=True).reshape(-1)
    served = pick_rows(asked, old_index).reshape(n_dp, CAP, e_local)
    back = lax.all_to_all(served, "dp", 0, 0, tiled=True).reshape(n_dp * CAP, e_local)
    old_vec = pick_rows(slot, back).reshape(rows, K, e_local)

    me_w = lax.axis_index("wide")
    right = [(i, (i + 1) % n_wide) for i in range(n_wide)]
    left = [(i, (i - 1) % n_wide) for i in range(n_wide)]

    blocks = {0: old_index}
    to_right, to_left = old_index, old_index
    for step in range(1, n_wide // 2 + 1):
        to_right = lax.ppermute(to_right, "wide", right)
        blocks[-step] = to_right
        if step < n_wide - n_wide // 2:
            to_left = lax.ppermute(to_left, "wide", left)
            blocks[step] = to_left
    offsets = sorted(blocks)
    old_full = jnp.concatenate([blocks[o] for o in offsets], axis=1)
    first = (me_w + offsets[0]) % n_wide
    rotated = lax.dynamic_slice_in_dim(
        jnp.concatenate([masked, masked], axis=1), first * e_local, width, 1
    )
    g_own = lax.dot_general(
        old_full, rotated, (((1,), (1,)), ((), ())), preferred_element_type=jnp.float32
    ).astype(jnp.bfloat16)
    served_g = pick_rows(asked, g_own).reshape(n_dp, CAP, e_local)
    back_g = lax.all_to_all(served_g, "dp", 0, 0, tiled=True).reshape(n_dp * CAP, e_local)
    g_vec = pick_rows(slot, back_g).reshape(rows, K, e_local).astype(jnp.float32)

    old_wide = old_vec.astype(jnp.float32)
    scale = 1.0 / math.sqrt(E)
    partial_scores = jnp.einsum("re,rke->rk", new, old_wide)
    spread = jnp.broadcast_to(partial_scores[None], (n_wide,) + partial_scores.shape)
    gathered = lax.all_to_all(spread, "wide", 0, 0, tiled=True)
    score = jnp.sum(gathered, axis=0) * scale
    sign = 2.0 * labels.astype(jnp.float32) - 1.0
    pair_loss = jax.nn.softplus(-sign * score)
    dscore = -sign * jax.nn.sigmoid(-sign * score)
    trunk_grad = jnp.einsum("rk,rke->re", dscore, g_vec) * scale
    return (new.astype(jnp.bfloat16), pair_loss, trunk_grad.astype(jnp.bfloat16))


def solution(mesh):
    n_dp, n_wide = mesh.shape["dp"], mesh.shape["wide"]
    return jax.shard_map(
        lambda *a: local(n_dp, n_wide, *a),
        mesh=mesh,
        in_specs=(
            P("dp", None),
            P(None, "wide"),
            P("wide", None),
            P("wide", None),
            P("dp", "wide"),
            P("dp", None),
            P("dp", None),
        ),
        out_specs=(P("dp", "wide"), P("dp", None), P("dp", "wide")),
        check_vma=False,
    )
```

```python
import math

import jax
import jax.numpy as jnp
from jax import lax
from jax.sharding import PartitionSpec as P

E = 4096
K = 4
CAP = 128


def one_hot(index, size, dtype=jnp.bfloat16):
    return (index[:, None] == jnp.arange(size, dtype=jnp.int32)[None, :]).astype(dtype)


def pick_rows(index, table):
    picked = jnp.dot(one_hot(index, table.shape[0]), table, preferred_element_type=jnp.float32)
    return picked.astype(table.dtype)


def local(n_dp, n_wide, trunk_out, projection, transform, block_mask, old_index, doc_ids, labels):
    rows = trunk_out.shape[0]
    e_local, width = transform.shape
    local_blocks, nblocks = block_mask.shape
    side = e_local // local_blocks
    doc_shard = old_index.shape[0]
    query = jnp.dot(trunk_out, projection, preferred_element_type=jnp.float32).astype(jnp.bfloat16)
    blocks = transform.reshape(local_blocks, side, nblocks, side)
    masked = (blocks * block_mask[:, None, :, None].astype(jnp.bfloat16)).reshape(e_local, width)
    term = jnp.dot(query, masked, preferred_element_type=jnp.float32)
    new = lax.psum_scatter(
        term.astype(jnp.bfloat16), "wide", scatter_dimension=1, tiled=True
    ).astype(jnp.float32)

    flat = doc_ids.reshape(-1)
    count = flat.shape[0]
    owner = flat // doc_shard
    loc = flat - owner * doc_shard
    by_owner = one_hot(owner, n_dp)
    ids = jnp.arange(count, dtype=jnp.int32)
    earlier = (ids[None, :] < ids[:, None]).astype(jnp.bfloat16)
    before = jnp.dot(earlier, by_owner, preferred_element_type=jnp.float32)
    rank = jnp.sum(before * by_owner.astype(jnp.float32), axis=1).astype(jnp.int32)
    slot = owner * CAP + rank
    by_rank = one_hot(rank, CAP)
    digits = jnp.stack([loc // 32, loc % 32], axis=0).astype(jnp.bfloat16)
    placed = jnp.einsum("di,io,ic->doc", digits, by_owner, by_rank,
                        preferred_element_type=jnp.float32).astype(jnp.int32)
    req = placed[0] * 32 + placed[1]
    asked = lax.all_to_all(req, "dp", 0, 0, tiled=True).reshape(-1)
    served = pick_rows(asked, old_index).reshape(n_dp, CAP, e_local)
    back = lax.all_to_all(served, "dp", 0, 0, tiled=True).reshape(n_dp * CAP, e_local)
    old_vec = pick_rows(slot, back).reshape(rows, K, e_local)

    me_w = lax.axis_index("wide")

    def place(full, block, source):
        return lax.dynamic_update_slice_in_dim(full, block, source * e_local, 1)

    old_full = place(jnp.zeros((doc_shard, width), old_index.dtype), old_index, me_w)
    quarter = n_wide // 4
    chains = [(1, 1, quarter), (-1, 1, quarter - 1), (1, quarter + 1, quarter), (-1, quarter, quarter)]
    for way, jump, length in chains:
        held, offset = old_index, 0
        for step in range(length):
            hop = jump if step == 0 else 1
            held = lax.ppermute(held, "wide", [(i, (i + way * hop) % n_wide) for i in range(n_wide)])
            offset += hop
            old_full = place(old_full, held, (me_w - way * offset) % n_wide)
    g_own = lax.dot_general(
        old_full, masked, (((1,), (1,)), ((), ())), preferred_element_type=jnp.float32
    ).astype(jnp.bfloat16)
    served_g = pick_rows(asked, g_own).reshape(n_dp, CAP, e_local)
    back_g = lax.all_to_all(served_g, "dp", 0, 0, tiled=True).reshape(n_dp * CAP, e_local)
    g_vec = pick_rows(slot, back_g).reshape(rows, K, e_local).astype(jnp.float32)

    old_wide = old_vec.astype(jnp.float32)
    scale = 1.0 / math.sqrt(E)
    partial_scores = jnp.einsum("re,rke->rk", new, old_wide)
    spread = jnp.broadcast_to(partial_scores[None], (n_wide,) + partial_scores.shape)
    gathered = lax.all_to_all(spread, "wide", 0, 0, tiled=True)
    score = jnp.sum(gathered, axis=0) * scale
    sign = 2.0 * labels.astype(jnp.float32) - 1.0
    pair_loss = jax.nn.softplus(-sign * score)
    dscore = -sign * jax.nn.sigmoid(-sign * score)
    trunk_grad = jnp.einsum("rk,rke->re", dscore, g_vec) * scale
    return (new.astype(jnp.bfloat16), pair_loss, trunk_grad.astype(jnp.bfloat16))


def solution(mesh):
    n_dp, n_wide = mesh.shape["dp"], mesh.shape["wide"]
    return jax.shard_map(
        lambda *a: local(n_dp, n_wide, *a),
        mesh=mesh,
        in_specs=(
            P("dp", None),
            P(None, "wide"),
            P("wide", None),
            P("wide", None),
            P("dp", "wide"),
            P("dp", None),
            P("dp", None),
        ),
        out_specs=(P("dp", "wide"), P("dp", None), P("dp", "wide")),
        check_vma=False,
    )
```

```python
import math

import jax
import jax.numpy as jnp
from jax import lax
from jax.sharding import PartitionSpec as P

E = 4096
K = 4
CAP = 128


def one_hot(index, size, dtype=jnp.bfloat16):
    return (index[:, None] == jnp.arange(size, dtype=jnp.int32)[None, :]).astype(dtype)


def pick_rows(index, table):
    picked = jnp.dot(one_hot(index, table.shape[0]), table, preferred_element_type=jnp.float32)
    return picked.astype(table.dtype)


def local(n_dp, n_wide, trunk_out, projection, transform, block_mask, old_index, doc_ids, labels):
    rows = trunk_out.shape[0]
    e_local, width = transform.shape
    local_blocks, nblocks = block_mask.shape
    side = e_local // local_blocks
    doc_shard = old_index.shape[0]
    blocks = transform.reshape(local_blocks, side, nblocks, side)
    masked = (blocks * block_mask[:, None, :, None].astype(jnp.bfloat16)).reshape(e_local, width)

    chunk = trunk_out.shape[1] // n_dp
    proj_rows = lax.dynamic_slice_in_dim(projection, lax.axis_index("dp") * chunk, chunk, 0)
    w_part = jnp.dot(proj_rows, masked, preferred_element_type=jnp.float32)
    w_parts = w_part.reshape(chunk, n_wide, e_local).transpose(1, 0, 2)
    w_blk = jnp.sum(lax.all_to_all(w_parts, "wide", 0, 0, tiled=True), axis=0)
    w_cols = lax.all_gather(w_blk.astype(jnp.bfloat16), "dp", axis=0, tiled=True)
    new = jnp.dot(trunk_out, w_cols, preferred_element_type=jnp.float32)

    flat = doc_ids.reshape(-1)
    count = flat.shape[0]
    owner = flat // doc_shard
    loc = flat - owner * doc_shard
    by_owner = one_hot(owner, n_dp)
    ids = jnp.arange(count, dtype=jnp.int32)
    earlier = (ids[None, :] < ids[:, None]).astype(jnp.bfloat16)
    before = jnp.dot(earlier, by_owner, preferred_element_type=jnp.float32)
    rank = jnp.sum(before * by_owner.astype(jnp.float32), axis=1).astype(jnp.int32)
    slot = owner * CAP + rank
    by_rank = one_hot(rank, CAP)
    digits = jnp.stack([loc // 32, loc % 32], axis=0).astype(jnp.bfloat16)
    placed = jnp.einsum("di,io,ic->doc", digits, by_owner, by_rank,
                        preferred_element_type=jnp.float32).astype(jnp.int32)
    req = placed[0] * 32 + placed[1]
    asked = lax.all_to_all(req, "dp", 0, 0, tiled=True).reshape(-1)
    served = pick_rows(asked, old_index).reshape(n_dp, CAP, e_local)
    back = lax.all_to_all(served, "dp", 0, 0, tiled=True).reshape(n_dp * CAP, e_local)
    old_vec = pick_rows(slot, back).reshape(rows, K, e_local)

    old_full = lax.all_gather(old_index, "wide", axis=1, tiled=True)
    g_own = lax.dot_general(
        old_full, masked, (((1,), (1,)), ((), ())), preferred_element_type=jnp.float32
    ).astype(jnp.bfloat16)
    served_g = pick_rows(asked, g_own).reshape(n_dp, CAP, e_local)
    back_g = lax.all_to_all(served_g, "dp", 0, 0, tiled=True).reshape(n_dp * CAP, e_local)
    g_vec = pick_rows(slot, back_g).reshape(rows, K, e_local).astype(jnp.float32)

    old_wide = old_vec.astype(jnp.float32)
    scale = 1.0 / math.sqrt(E)
    partial_scores = jnp.einsum("re,rke->rk", new, old_wide)
    spread = jnp.broadcast_to(partial_scores[None], (n_wide,) + partial_scores.shape)
    gathered = lax.all_to_all(spread, "wide", 0, 0, tiled=True)
    score = jnp.sum(gathered, axis=0) * scale
    sign = 2.0 * labels.astype(jnp.float32) - 1.0
    pair_loss = jax.nn.softplus(-sign * score)
    dscore = -sign * jax.nn.sigmoid(-sign * score)
    trunk_grad = jnp.einsum("rk,rke->re", dscore, g_vec) * scale
    return (new.astype(jnp.bfloat16), pair_loss, trunk_grad.astype(jnp.bfloat16))


def solution(mesh):
    n_dp, n_wide = mesh.shape["dp"], mesh.shape["wide"]
    return jax.shard_map(
        lambda *a: local(n_dp, n_wide, *a),
        mesh=mesh,
        in_specs=(
            P("dp", None),
            P(None, "wide"),
            P("wide", None),
            P("wide", None),
            P("dp", "wide"),
            P("dp", None),
            P("dp", None),
        ),
        out_specs=(P("dp", "wide"), P("dp", None), P("dp", "wide")),
        check_vma=False,
    )
```

```python
import math

import jax
import jax.numpy as jnp
from jax import lax
from jax.sharding import PartitionSpec as P

E = 4096
K = 4
CAP = 128


def one_hot(index, size, dtype=jnp.bfloat16):
    return (index[:, None] == jnp.arange(size, dtype=jnp.int32)[None, :]).astype(dtype)


def pick_rows(index, table):
    picked = jnp.dot(one_hot(index, table.shape[0]), table, preferred_element_type=jnp.float32)
    return picked.astype(table.dtype)


def local(n_dp, n_wide, trunk_out, projection, transform, block_mask, old_index, doc_ids, labels):
    rows = trunk_out.shape[0]
    e_local, width = transform.shape
    local_blocks, nblocks = block_mask.shape
    side = e_local // local_blocks
    doc_shard = old_index.shape[0]
    query = jnp.dot(trunk_out, projection, preferred_element_type=jnp.float32).astype(jnp.bfloat16)
    blocks = transform.reshape(local_blocks, side, nblocks, side)
    masked = (blocks * block_mask[:, None, :, None].astype(jnp.bfloat16)).reshape(e_local, width)
    term = jnp.dot(query, masked, preferred_element_type=jnp.float32)
    new = lax.psum_scatter(
        term.astype(jnp.bfloat16), "wide", scatter_dimension=1, tiled=True
    ).astype(jnp.float32)

    flat = doc_ids.reshape(-1)
    count = flat.shape[0]
    owner = flat // doc_shard
    loc = flat - owner * doc_shard
    by_owner = one_hot(owner, n_dp)
    ids = jnp.arange(count, dtype=jnp.int32)
    earlier = (ids[None, :] < ids[:, None]).astype(jnp.bfloat16)
    before = jnp.dot(earlier, by_owner, preferred_element_type=jnp.float32)
    rank = jnp.sum(before * by_owner.astype(jnp.float32), axis=1).astype(jnp.int32)
    slot = owner * CAP + rank
    by_rank = one_hot(rank, CAP)
    digits = jnp.stack([loc // 32, loc % 32], axis=0).astype(jnp.bfloat16)
    placed = jnp.einsum("di,io,ic->doc", digits, by_owner, by_rank,
                        preferred_element_type=jnp.float32).astype(jnp.int32)
    req = placed[0] * 32 + placed[1]
    asked = lax.all_to_all(req, "dp", 0, 0, tiled=True).reshape(-1)
    served = pick_rows(asked, old_index).reshape(n_dp, CAP, e_local)
    back = lax.all_to_all(served, "dp", 0, 0, tiled=True).reshape(n_dp * CAP, e_local)
    old_vec = pick_rows(slot, back).reshape(rows, K, e_local)

    me_w = lax.axis_index("wide")
    right = [(i, (i + 1) % n_wide) for i in range(n_wide)]
    left = [(i, (i - 1) % n_wide) for i in range(n_wide)]

    def place(full, block, source):
        return lax.dynamic_update_slice_in_dim(full, block, source * e_local, 1)

    old_full = place(jnp.zeros((doc_shard, width), old_index.dtype), old_index, me_w)
    to_right, to_left = old_index, old_index
    for step in range(1, n_wide // 2 + 1):
        to_right = lax.ppermute(to_right, "wide", right)
        old_full = place(old_full, to_right, (me_w - step) % n_wide)
        if step < n_wide - n_wide // 2:
            to_left = lax.ppermute(to_left, "wide", left)
            old_full = place(old_full, to_left, (me_w + step) % n_wide)
    g_own = lax.dot_general(
        old_full, masked, (((1,), (1,)), ((), ())), preferred_element_type=jnp.float32
    ).astype(jnp.bfloat16)
    served_g = pick_rows(asked, g_own).reshape(n_dp, CAP, e_local)
    back_g = lax.all_to_all(served_g, "dp", 0, 0, tiled=True).reshape(n_dp * CAP, e_local)

    old_wide = old_vec.astype(jnp.float32)
    scale = 1.0 / math.sqrt(E)
    partial_scores = jnp.einsum("re,rke->rk", new, old_wide)
    score = lax.psum(partial_scores, "wide") * scale
    sign = 2.0 * labels.astype(jnp.float32) - 1.0
    pair_loss = jax.nn.softplus(-sign * score)
    dscore = -sign * jax.nn.sigmoid(-sign * score)
    by_slot = slot.reshape(rows, K)[:, :, None] == jnp.arange(n_dp * CAP, dtype=jnp.int32)
    weights = jnp.sum(jnp.where(by_slot, dscore[:, :, None], 0.0), axis=1)
    high = weights.astype(jnp.bfloat16)
    low = (weights - high.astype(jnp.float32)).astype(jnp.bfloat16)
    trunk_grad = (
        jnp.dot(high, back_g, preferred_element_type=jnp.float32)
        + jnp.dot(low, back_g, preferred_element_type=jnp.float32)
    ) * scale
    return (new.astype(jnp.bfloat16), pair_loss, trunk_grad.astype(jnp.bfloat16))


def solution(mesh):
    n_dp, n_wide = mesh.shape["dp"], mesh.shape["wide"]
    return jax.shard_map(
        lambda *a: local(n_dp, n_wide, *a),
        mesh=mesh,
        in_specs=(
            P("dp", None),
            P(None, "wide"),
            P("wide", None),
            P("wide", None),
            P("dp", "wide"),
            P("dp", None),
            P("dp", None),
        ),
        out_specs=(P("dp", "wide"), P("dp", None), P("dp", "wide")),
        check_vma=False,
    )
```

```python
import math

import jax
import jax.numpy as jnp
from jax import lax
from jax.sharding import PartitionSpec as P

E = 4096
K = 4
CAP = 128


def one_hot(index, size, dtype=jnp.bfloat16):
    return (index[:, None] == jnp.arange(size, dtype=jnp.int32)[None, :]).astype(dtype)


def pick_rows(index, table):
    picked = jnp.dot(one_hot(index, table.shape[0]), table, preferred_element_type=jnp.float32)
    return picked.astype(table.dtype)


def local(n_dp, n_wide, trunk_out, projection, transform, block_mask, old_index, doc_ids, labels):
    rows = trunk_out.shape[0]
    e_local, width = transform.shape
    local_blocks, nblocks = block_mask.shape
    side = e_local // local_blocks
    doc_shard = old_index.shape[0]
    query = jnp.dot(trunk_out, projection, preferred_element_type=jnp.float32).astype(jnp.bfloat16)
    blocks = transform.reshape(local_blocks, side, nblocks, side)
    masked = (blocks * block_mask[:, None, :, None].astype(jnp.bfloat16)).reshape(e_local, width)
    term = jnp.dot(query, masked, preferred_element_type=jnp.float32).astype(jnp.bfloat16)

    me_w = lax.axis_index("wide")
    right = [(i, (i + 1) % n_wide) for i in range(n_wide)]
    left = [(i, (i - 1) % n_wide) for i in range(n_wide)]

    def part(block):
        return lax.dynamic_slice_in_dim(term, (block % n_wide) * e_local, e_local, 1)

    far_r, far_l = n_wide // 2, n_wide - 1 - n_wide // 2
    run_r, run_l = part(me_w + far_r), part(me_w - far_l)
    for step in range(1, far_r + 1):
        run_r = lax.ppermute(run_r, "wide", right)
        if step < far_r:
            run_r = (run_r.astype(jnp.float32) + part(me_w - step + far_r)).astype(jnp.bfloat16)
        if step <= far_l:
            run_l = lax.ppermute(run_l, "wide", left)
            if step < far_l:
                run_l = (run_l.astype(jnp.float32) + part(me_w + step - far_l)).astype(jnp.bfloat16)
    new = run_r.astype(jnp.float32) + run_l.astype(jnp.float32) + part(me_w).astype(jnp.float32)

    flat = doc_ids.reshape(-1)
    count = flat.shape[0]
    owner = flat // doc_shard
    loc = flat - owner * doc_shard
    by_owner = one_hot(owner, n_dp)
    ids = jnp.arange(count, dtype=jnp.int32)
    earlier = (ids[None, :] < ids[:, None]).astype(jnp.bfloat16)
    before = jnp.dot(earlier, by_owner, preferred_element_type=jnp.float32)
    rank = jnp.sum(before * by_owner.astype(jnp.float32), axis=1).astype(jnp.int32)
    slot = owner * CAP + rank
    by_rank = one_hot(rank, CAP)
    digits = jnp.stack([loc // 32, loc % 32], axis=0).astype(jnp.bfloat16)
    placed = jnp.einsum("di,io,ic->doc", digits, by_owner, by_rank,
                        preferred_element_type=jnp.float32).astype(jnp.int32)
    req = placed[0] * 32 + placed[1]
    asked = lax.all_to_all(req, "dp", 0, 0, tiled=True).reshape(-1)
    served = pick_rows(asked, old_index).reshape(n_dp, CAP, e_local)
    back = lax.all_to_all(served, "dp", 0, 0, tiled=True).reshape(n_dp * CAP, e_local)
    old_vec = pick_rows(slot, back).reshape(rows, K, e_local)

    old_full = lax.all_gather(old_index, "wide", axis=1, tiled=True)
    g_own = lax.dot_general(
        old_full, masked, (((1,), (1,)), ((), ())), preferred_element_type=jnp.float32
    ).astype(jnp.bfloat16)
    served_g = pick_rows(asked, g_own).reshape(n_dp, CAP, e_local)
    back_g = lax.all_to_all(served_g, "dp", 0, 0, tiled=True).reshape(n_dp * CAP, e_local)
    g_vec = pick_rows(slot, back_g).reshape(rows, K, e_local).astype(jnp.float32)

    old_wide = old_vec.astype(jnp.float32)
    scale = 1.0 / math.sqrt(E)
    partial_scores = jnp.einsum("re,rke->rk", new, old_wide)
    spread = jnp.broadcast_to(partial_scores[None], (n_wide,) + partial_scores.shape)
    gathered = lax.all_to_all(spread, "wide", 0, 0, tiled=True)
    score = jnp.sum(gathered, axis=0) * scale
    sign = 2.0 * labels.astype(jnp.float32) - 1.0
    pair_loss = jax.nn.softplus(-sign * score)
    dscore = -sign * jax.nn.sigmoid(-sign * score)
    trunk_grad = jnp.einsum("rk,rke->re", dscore, g_vec) * scale
    return (new.astype(jnp.bfloat16), pair_loss, trunk_grad.astype(jnp.bfloat16))


def solution(mesh):
    n_dp, n_wide = mesh.shape["dp"], mesh.shape["wide"]
    return jax.shard_map(
        lambda *a: local(n_dp, n_wide, *a),
        mesh=mesh,
        in_specs=(
            P("dp", None),
            P(None, "wide"),
            P("wide", None),
            P("wide", None),
            P("dp", "wide"),
            P("dp", None),
            P("dp", None),
        ),
        out_specs=(P("dp", "wide"), P("dp", None), P("dp", "wide")),
        check_vma=False,
    )
```

```python
import math

import jax
import jax.numpy as jnp
from jax import lax
from jax.sharding import PartitionSpec as P

E = 4096
K = 4
CAP = 128


def one_hot(index, size, dtype=jnp.bfloat16):
    return (index[:, None] == jnp.arange(size, dtype=jnp.int32)[None, :]).astype(dtype)


def pick_rows(index, table):
    picked = jnp.dot(one_hot(index, table.shape[0]), table, preferred_element_type=jnp.float32)
    return picked.astype(table.dtype)


def local(n_dp, n_wide, trunk_out, projection, transform, block_mask, old_index, doc_ids, labels):
    rows = trunk_out.shape[0]
    e_local, width = transform.shape
    local_blocks, nblocks = block_mask.shape
    side = e_local // local_blocks
    doc_shard = old_index.shape[0]
    query = jnp.dot(trunk_out, projection, preferred_element_type=jnp.float32).astype(jnp.bfloat16)
    blocks = transform.reshape(local_blocks, side, nblocks, side)
    masked = (blocks * block_mask[:, None, :, None].astype(jnp.bfloat16)).reshape(e_local, width)
    term = jnp.dot(query, masked, preferred_element_type=jnp.float32)
    new = lax.psum_scatter(
        term.astype(jnp.bfloat16), "wide", scatter_dimension=1, tiled=True
    ).astype(jnp.float32)

    flat = doc_ids.reshape(-1)
    count = flat.shape[0]
    owner = flat // doc_shard
    loc = flat - owner * doc_shard
    by_owner = one_hot(owner, n_dp)
    ids = jnp.arange(count, dtype=jnp.int32)
    earlier = (ids[None, :] < ids[:, None]).astype(jnp.bfloat16)
    before = jnp.dot(earlier, by_owner, preferred_element_type=jnp.float32)
    rank = jnp.sum(before * by_owner.astype(jnp.float32), axis=1).astype(jnp.int32)
    slot = owner * CAP + rank
    by_rank = one_hot(rank, CAP)
    digits = jnp.stack([loc // 32, loc % 32], axis=0).astype(jnp.bfloat16)
    placed = jnp.einsum("di,io,ic->doc", digits, by_owner, by_rank,
                        preferred_element_type=jnp.float32).astype(jnp.int32)
    req = placed[0] * 32 + placed[1]
    asked = lax.all_to_all(req, "dp", 0, 0, tiled=True).reshape(-1)
    served = pick_rows(asked, old_index).reshape(n_dp, CAP, e_local)
    back = lax.all_to_all(served, "dp", 0, 0, tiled=True).reshape(n_dp * CAP, e_local)
    old_vec = pick_rows(slot, back).reshape(rows, K, e_local)

    me_w = lax.axis_index("wide")
    right = [(i, (i + 1) % n_wide) for i in range(n_wide)]
    left = [(i, (i - 1) % n_wide) for i in range(n_wide)]

    def place(full, block, source):
        return lax.dynamic_update_slice_in_dim(full, block, source * e_local, 1)

    old_full = place(jnp.zeros((doc_shard, width), old_index.dtype), old_index, me_w)
    to_right, to_left = old_index, old_index
    for step in range(1, n_wide // 2 + 1):
        to_right = lax.ppermute(to_right, "wide", right)
        old_full = place(old_full, to_right, (me_w - step) % n_wide)
        if step < n_wide - n_wide // 2:
            to_left = lax.ppermute(to_left, "wide", left)
            old_full = place(old_full, to_left, (me_w + step) % n_wide)
    g_own = lax.dot_general(
        old_full, masked, (((1,), (1,)), ((), ())), preferred_element_type=jnp.float32
    ).astype(jnp.bfloat16)
    served_g = pick_rows(asked, g_own).reshape(n_dp, CAP, e_local)
    back_g = lax.all_to_all(served_g, "dp", 0, 0, tiled=True).reshape(n_dp * CAP, e_local)

    old_wide = old_vec.astype(jnp.float32)
    scale = 1.0 / math.sqrt(E)
    partial_scores = jnp.einsum("re,rke->rk", new, old_wide)
    score = lax.psum(partial_scores, "wide") * scale
    back_g, score = lax.optimization_barrier((back_g, score))
    g_vec = pick_rows(slot, back_g).reshape(rows, K, e_local).astype(jnp.float32)
    sign = 2.0 * labels.astype(jnp.float32) - 1.0
    pair_loss = jax.nn.softplus(-sign * score)
    dscore = -sign * jax.nn.sigmoid(-sign * score)
    trunk_grad = jnp.einsum("rk,rke->re", dscore, g_vec) * scale
    return (new.astype(jnp.bfloat16), pair_loss, trunk_grad.astype(jnp.bfloat16))


def solution(mesh):
    n_dp, n_wide = mesh.shape["dp"], mesh.shape["wide"]
    return jax.shard_map(
        lambda *a: local(n_dp, n_wide, *a),
        mesh=mesh,
        in_specs=(
            P("dp", None),
            P(None, "wide"),
            P("wide", None),
            P("wide", None),
            P("dp", "wide"),
            P("dp", None),
            P("dp", None),
        ),
        out_specs=(P("dp", "wide"), P("dp", None), P("dp", "wide")),
        check_vma=False,
    )
```

```python
import math

import jax
import jax.numpy as jnp
from jax import lax
from jax.sharding import PartitionSpec as P

E = 4096
K = 4
CAP = 128


def one_hot(index, size, dtype=jnp.bfloat16):
    return (index[:, None] == jnp.arange(size, dtype=jnp.int32)[None, :]).astype(dtype)


def pick_rows(index, table):
    picked = jnp.dot(one_hot(index, table.shape[0]), table, preferred_element_type=jnp.float32)
    return picked.astype(table.dtype)


def local(n_dp, n_wide, trunk_out, projection, transform, block_mask, old_index, doc_ids, labels):
    rows = trunk_out.shape[0]
    e_local, width = transform.shape
    local_blocks, nblocks = block_mask.shape
    side = e_local // local_blocks
    doc_shard = old_index.shape[0]
    query = jnp.dot(trunk_out, projection, preferred_element_type=jnp.float32).astype(jnp.bfloat16)
    blocks = transform.reshape(local_blocks, side, nblocks, side)
    masked = (blocks * block_mask[:, None, :, None].astype(jnp.bfloat16)).reshape(e_local, width)
    term = jnp.dot(query, masked, preferred_element_type=jnp.float32)
    new = lax.psum_scatter(
        term.astype(jnp.bfloat16), "wide", scatter_dimension=1, tiled=True
    ).astype(jnp.float32)

    flat = doc_ids.reshape(-1)
    count = flat.shape[0]
    owner = flat // doc_shard
    loc = flat - owner * doc_shard
    by_owner = one_hot(owner, n_dp)
    ids = jnp.arange(count, dtype=jnp.int32)
    earlier = (ids[None, :] < ids[:, None]).astype(jnp.bfloat16)
    before = jnp.dot(earlier, by_owner, preferred_element_type=jnp.float32)
    rank = jnp.sum(before * by_owner.astype(jnp.float32), axis=1).astype(jnp.int32)
    slot = owner * CAP + rank
    by_rank = one_hot(rank, CAP)
    digits = jnp.stack([loc // 32, loc % 32], axis=0).astype(jnp.bfloat16)
    placed = jnp.einsum("di,io,ic->doc", digits, by_owner, by_rank,
                        preferred_element_type=jnp.float32).astype(jnp.int32)
    req = placed[0] * 32 + placed[1]
    asked = lax.all_to_all(req, "dp", 0, 0, tiled=True).reshape(-1)
    served = pick_rows(asked, old_index).reshape(n_dp, CAP, e_local)
    back = lax.all_to_all(served, "dp", 0, 0, tiled=True).reshape(n_dp * CAP, e_local)
    by_k = slot.reshape(rows, K).T.reshape(-1)
    old_vec = pick_rows(by_k, back).reshape(K, rows, e_local)

    me_w = lax.axis_index("wide")
    right = [(i, (i + 1) % n_wide) for i in range(n_wide)]
    left = [(i, (i - 1) % n_wide) for i in range(n_wide)]

    def place(full, block, source):
        return lax.dynamic_update_slice_in_dim(full, block, source * e_local, 1)

    old_full = place(jnp.zeros((doc_shard, width), old_index.dtype), old_index, me_w)
    to_right, to_left = old_index, old_index
    for step in range(1, n_wide // 2 + 1):
        to_right = lax.ppermute(to_right, "wide", right)
        old_full = place(old_full, to_right, (me_w - step) % n_wide)
        if step < n_wide - n_wide // 2:
            to_left = lax.ppermute(to_left, "wide", left)
            old_full = place(old_full, to_left, (me_w + step) % n_wide)
    g_own = lax.dot_general(
        old_full, masked, (((1,), (1,)), ((), ())), preferred_element_type=jnp.float32
    ).astype(jnp.bfloat16)
    served_g = pick_rows(asked, g_own).reshape(n_dp, CAP, e_local)
    back_g = lax.all_to_all(served_g, "dp", 0, 0, tiled=True).reshape(n_dp * CAP, e_local)

    old_wide = old_vec.astype(jnp.float32)
    scale = 1.0 / math.sqrt(E)
    partial_scores = jnp.einsum("re,kre->rk", new, old_wide)
    score = lax.psum(partial_scores, "wide") * scale
    back_g, score = lax.optimization_barrier((back_g, score))
    g_vec = pick_rows(by_k, back_g).reshape(K, rows, e_local).astype(jnp.float32)
    sign = 2.0 * labels.astype(jnp.float32) - 1.0
    pair_loss = jax.nn.softplus(-sign * score)
    dscore = -sign * jax.nn.sigmoid(-sign * score)
    trunk_grad = jnp.einsum("rk,kre->re", dscore, g_vec) * scale
    return (new.astype(jnp.bfloat16), pair_loss, trunk_grad.astype(jnp.bfloat16))


def solution(mesh):
    n_dp, n_wide = mesh.shape["dp"], mesh.shape["wide"]
    return jax.shard_map(
        lambda *a: local(n_dp, n_wide, *a),
        mesh=mesh,
        in_specs=(
            P("dp", None),
            P(None, "wide"),
            P("wide", None),
            P("wide", None),
            P("dp", "wide"),
            P("dp", None),
            P("dp", None),
        ),
        out_specs=(P("dp", "wide"), P("dp", None), P("dp", "wide")),
        check_vma=False,
    )
```

```python
import math

import jax
import jax.numpy as jnp
from jax import lax
from jax.sharding import PartitionSpec as P

E = 4096
K = 4
CAP = 128


def one_hot(index, size, dtype=jnp.bfloat16):
    return (index[:, None] == jnp.arange(size, dtype=jnp.int32)[None, :]).astype(dtype)


def pick_rows(index, table):
    picked = jnp.dot(one_hot(index, table.shape[0]), table, preferred_element_type=jnp.float32)
    return picked.astype(table.dtype)


def local(n_dp, n_wide, trunk_out, projection, transform, block_mask, old_index, doc_ids, labels):
    rows = trunk_out.shape[0]
    e_local, width = transform.shape
    local_blocks, nblocks = block_mask.shape
    side = e_local // local_blocks
    doc_shard = old_index.shape[0]
    query = jnp.dot(trunk_out, projection, preferred_element_type=jnp.float32).astype(jnp.bfloat16)
    blocks = transform.reshape(local_blocks, side, nblocks, side)
    masked = (blocks * block_mask[:, None, :, None].astype(jnp.bfloat16)).reshape(e_local, width)
    term = jnp.dot(query, masked, preferred_element_type=jnp.float32)
    new = lax.psum_scatter(
        term.astype(jnp.bfloat16), "wide", scatter_dimension=1, tiled=True
    ).astype(jnp.float32)

    flat = doc_ids.reshape(-1)
    count = flat.shape[0]
    owner = flat // doc_shard
    loc = flat - owner * doc_shard
    by_owner = one_hot(owner, n_dp)
    ids = jnp.arange(count, dtype=jnp.int32)
    earlier = (ids[None, :] < ids[:, None]).astype(jnp.bfloat16)
    before = jnp.dot(earlier, by_owner, preferred_element_type=jnp.float32)
    rank = jnp.sum(before * by_owner.astype(jnp.float32), axis=1).astype(jnp.int32)
    slot = owner * CAP + rank
    by_rank = one_hot(rank, CAP)
    digits = jnp.stack([loc // 32, loc % 32], axis=0).astype(jnp.bfloat16)
    placed = jnp.einsum("di,io,ic->doc", digits, by_owner, by_rank,
                        preferred_element_type=jnp.float32).astype(jnp.int32)
    req = placed[0] * 32 + placed[1]
    asked = lax.all_to_all(req, "dp", 0, 0, tiled=True).reshape(-1)
    served = pick_rows(asked, old_index).reshape(n_dp, CAP, e_local)
    back = lax.all_to_all(served, "dp", 0, 0, tiled=True).reshape(n_dp * CAP, e_local)
    old_vec = pick_rows(slot, back).reshape(rows, K, e_local)

    me_w = lax.axis_index("wide")
    right = [(i, (i + 1) % n_wide) for i in range(n_wide)]
    left = [(i, (i - 1) % n_wide) for i in range(n_wide)]

    def place(full, block, source):
        return lax.dynamic_update_slice_in_dim(full, block, source * e_local, 1)

    old_full = place(jnp.zeros((doc_shard, width), old_index.dtype), old_index, me_w)
    to_right, to_left = old_index, old_index
    for step in range(1, n_wide // 2 + 1):
        if step == n_wide // 2 - 1:
            old_vec, to_right = lax.optimization_barrier((old_vec, to_right))
        to_right = lax.ppermute(to_right, "wide", right)
        old_full = place(old_full, to_right, (me_w - step) % n_wide)
        if step < n_wide - n_wide // 2:
            to_left = lax.ppermute(to_left, "wide", left)
            old_full = place(old_full, to_left, (me_w + step) % n_wide)
    g_own = lax.dot_general(
        old_full, masked, (((1,), (1,)), ((), ())), preferred_element_type=jnp.float32
    ).astype(jnp.bfloat16)
    served_g = pick_rows(asked, g_own).reshape(n_dp, CAP, e_local)
    back_g = lax.all_to_all(served_g, "dp", 0, 0, tiled=True).reshape(n_dp * CAP, e_local)

    old_wide = old_vec.astype(jnp.float32)
    scale = 1.0 / math.sqrt(E)
    partial_scores = jnp.einsum("re,rke->rk", new, old_wide)
    score = lax.psum(partial_scores, "wide") * scale
    back_g, score = lax.optimization_barrier((back_g, score))
    g_vec = pick_rows(slot, back_g).reshape(rows, K, e_local).astype(jnp.float32)
    sign = 2.0 * labels.astype(jnp.float32) - 1.0
    pair_loss = jax.nn.softplus(-sign * score)
    dscore = -sign * jax.nn.sigmoid(-sign * score)
    trunk_grad = jnp.einsum("rk,rke->re", dscore, g_vec) * scale
    return (new.astype(jnp.bfloat16), pair_loss, trunk_grad.astype(jnp.bfloat16))


def solution(mesh):
    n_dp, n_wide = mesh.shape["dp"], mesh.shape["wide"]
    return jax.shard_map(
        lambda *a: local(n_dp, n_wide, *a),
        mesh=mesh,
        in_specs=(
            P("dp", None),
            P(None, "wide"),
            P("wide", None),
            P("wide", None),
            P("dp", "wide"),
            P("dp", None),
            P("dp", None),
        ),
        out_specs=(P("dp", "wide"), P("dp", None), P("dp", "wide")),
        check_vma=False,
    )
```
